1024 devices in a mesh: ctx: 64 (over z, core), exp: 16 (over x, y).
Axes of the slice: x: 4, y: 4, z: 32, core: 2. Of those that a mesh axis runs over, the one named last changes fastest.
Arguments:
- route_ids: int32 [8192, 8], P('ctx'), may hold values from 0 to 255, all different within a row; in each aligned block of 128 rows (0 to 127, 128 to 255, ...) at most 6 rows name the same one
- route_probs: float32 [8192, 8], P('ctx'), may hold values from 0.02 to 0.4
- moe_grad: bfloat16 [8192, 2304], P('ctx'), may hold values from -6 to 6
- saved_gate: bfloat16 [1024, 64, 6, 256], P(('ctx', 'exp')), may hold values from -6 to 6
- saved_up: bfloat16 [1024, 64, 6, 256], P(('ctx', 'exp')), may hold values from -6 to 6
- w_up: bfloat16 [1024, 2304, 256], P(('ctx', 'exp')), may hold values from -0.125 to 0.125
- w_down: bfloat16 [1024, 256, 2304], P(('ctx', 'exp')), may hold values from -0.1875 to 0.1875
- conv_grad: bfloat16 [8192, 4096], P('ctx', 'exp'), may hold values from -6 to 6
- conv_pre: bfloat16 [8192, 4096], P('ctx', 'exp'), may hold values from -6 to 6
- conv_kernel: float32 [4, 4096], P(None, 'exp'), may hold values from -3 to 3
- w_key: bfloat16 [2304, 4096], P('exp'), may hold values from -0.125 to 0.125
Outputs:
- input_grad: float32 [8192, 2304], P('ctx', 'exp')
- gate_grad: bfloat16 [1024, 64, 6, 256], P(('ctx', 'exp'))
The draws below stay inside these ranges and needn't reach their ends.
Inputs may be any that keep to these rules, and one draw needn't show every extreme that they name: `route_ids`: each row names 8 different experts. Among the rows of one index of ctx (128 rows in a row) no expert is named more than 6 times, and in every draw some expert is named exactly 6 times by the rows of some index of ctx.
All inputs are finite; a program needn't handle non-finite values.
Results may differ from the reference program's by a relative error of at most 0.0095.
Values may be sent and summed in bfloat16 or wider, within the bound.
No kernel may reach another device: no remote copies, remote signals or barrier semaphores. Data moves between devices by JAX's collectives and lax.ppermute only.
A program may use at most 32 MiB of HBM per device.

```python
import math
import jax
import jax.numpy as jnp
import numpy as np
from jax import lax

D = 2304
FF = 1024
TOP = 8
CONV = 4096
KERNEL = 4
SPLIT = 4
TOK_C = 128
TOKENS = 8192
EXPERTS = 256
CAP = 6
FF_DEV = 256
N_CTX = 64


def steps_of(stream_key, extent, pieces, smallest, top_value):
    loudness, own = 1.0, jax.random.fold_in(stream_key, 6)
    for position, shards_of in pieces:
        draws = jnp.exp(jax.random.uniform(jax.random.fold_in(own, position), (shards_of,), jnp.float32, smallest / len(pieces), top_value / len(pieces)))
        loudness = loudness * jnp.repeat(draws, extent[position] // shards_of).reshape([-1 if axis == position else 1 for axis in range(len(extent))])
    return loudness


def routed_block(stream_key, own, number, rows, count, top, most, slope):
    ranking = jax.random.permutation(stream_key, count)
    packed, ordinary = load_shares(count, rows * top, most, slope, True), load_shares(count, rows * top, most, slope, False)
    places = jnp.arange(count)

    def named(tallies, rotation):
        used = int((tallies > 0).sum())
        fixed = max(1, used // 4)
        passed = fixed + (places - fixed + rotation * (used - fixed)) % max(1, count - fixed)
        return jnp.zeros((count,), jnp.int32).at[ranking[jnp.where(places < fixed, places, passed)]].set(jnp.asarray(tallies, jnp.int32))

    tallies = jnp.where(number % 4 == 0, named(packed, number // 4), named(ordinary, number - number // 4 - 1))
    mixed = jax.random.permutation(jax.random.fold_in(own, 3), count)
    donor, sink = mixed[0:count // 2 * 2:2], mixed[1:count // 2 * 2:2]
    room = jnp.minimum(tallies[donor] - 1, most - tallies[sink]) // 2
    room = jnp.where((donor == ranking[0]) | (sink == ranking[0]) | (tallies[sink] == 0), 0, jnp.maximum(room, 0))
    passed = jax.random.randint(jax.random.fold_in(own, 4), (count // 2,), 0, 1 << 20) % (room + 1)
    tallies = tallies.at[donor].add(-passed).at[sink].add(passed)
    members = jnp.searchsorted(jnp.cumsum(tallies), jnp.arange(rows * top), side="right").astype(jnp.int32)
    table = members.reshape(top, rows).T
    table = table[jax.random.permutation(jax.random.fold_in(own, 1), rows)]
    rotation = jax.random.randint(jax.random.fold_in(own, 2), (rows, 1), 0, top)
    return jnp.take_along_axis(table, (jnp.arange(top)[None, :] + rotation) % top, axis=1)


def load_shares(number_of, total, bound, slope, full):
    weights = [(1 << 20) // math.isqrt(rank ** slope) + 1 for rank in range(1, number_of + 1)]
    largest = bound if full else min(bound, max(-(-total // number_of), total * weights[0] // sum(weights)))
    least = 1 if total - largest >= number_of - 1 else 0
    holding, rest = [largest] + [least] * (number_of - 1), total - largest - least * (number_of - 1)
    while rest > 0:
        candidates = [i for i in range(1, number_of) if holding[i] < largest] or [i for i in range(1, number_of) if holding[i] < bound]
        whole, remaining = sum([weights[i] for i in candidates]), rest
        for i in candidates:
            addition = min(bound - holding[i], max(1, remaining * weights[i] // whole), rest)
            holding[i] = holding[i] + addition
            rest = rest - addition
    return np.array(holding)


def noise(key, extent, spread, most, cuts=(), kind=jnp.bfloat16):
    loudness = steps_of(key, extent, cuts, -0.22, 0.18) if cuts else 1.0
    drawn = jax.random.normal(key, extent, jnp.float32) * spread * loudness
    return jnp.minimum(jnp.maximum(drawn, -most), most).astype(kind)


def setup_inputs(seed: int = 0) -> dict:
    keys = jax.random.split(jax.random.key(seed), 12)
    route_ids_keys = jax.random.split(jax.random.fold_in(keys[0], 1), TOKENS // TOK_C)
    route_ids_turns = jax.random.permutation(jax.random.fold_in(keys[0], 3), TOKENS // TOK_C)
    route_ids = jax.vmap(lambda own, number: routed_block(jax.random.fold_in(keys[0], 2), own, number, TOK_C, EXPERTS, TOP, CAP, 2))(route_ids_keys, route_ids_turns).reshape((TOKENS, TOP))
    route_probs = jnp.clip(0.02 + 0.38 * jax.random.uniform(keys[1], (TOKENS, TOP), jnp.float32) ** steps_of(keys[1], (TOKENS, TOP), ((0, 64),), -0.2, 0.2), 0.02, 0.4)
    moe_grad = noise(keys[2], (TOKENS, D), 1.0, 6.0, ((0, 64),))
    saved_gate = noise(keys[3], (EXPERTS * SPLIT, N_CTX, CAP, FF_DEV), 1.5, 6.0, ((0, 1024),))
    saved_up = noise(keys[4], (EXPERTS * SPLIT, N_CTX, CAP, FF_DEV), 1.0, 6.0, ((0, 1024),))
    w_up = noise(keys[5], (EXPERTS * SPLIT, D, FF_DEV), D ** -0.5, 0.125, ((0, 1024),))
    w_down = noise(keys[6], (EXPERTS * SPLIT, FF_DEV, D), FF ** -0.5, 0.1875, ((0, 1024),))
    conv_grad = noise(keys[7], (TOKENS, CONV), 1.0, 6.0, ((0, 64), (1, 16)))
    conv_pre = noise(keys[8], (TOKENS, CONV), 1.5, 6.0, ((0, 64), (1, 16)))
    conv_kernel = noise(keys[9], (KERNEL, CONV), 0.5, 3.0, ((1, 16),), jnp.float32)
    w_key = noise(keys[10], (D, CONV), D ** -0.5, 0.125, ((0, 16),))
    return dict(route_ids=route_ids, route_probs=route_probs, moe_grad=moe_grad, saved_gate=saved_gate, saved_up=saved_up, w_up=w_up, w_down=w_down, conv_grad=conv_grad, conv_pre=conv_pre, conv_kernel=conv_kernel, w_key=w_key)


def silu_slope(values):
    logistic = jax.nn.sigmoid(values)
    return logistic * (1.0 + values * (1.0 - logistic))


def reference(route_ids, route_probs, moe_grad, saved_gate, saved_up, w_up, w_down, conv_grad, conv_pre, conv_kernel, w_key):
    grad_pre = conv_grad.astype(jnp.float32) * silu_slope(conv_pre.astype(jnp.float32))
    extended = jnp.concatenate([grad_pre, jnp.zeros((KERNEL - 1, CONV), grad_pre.dtype)], 0)
    key_sum = conv_kernel[0][None, :] * extended[0:TOKENS]
    for offset in range(1, KERNEL):
        key_sum = key_sum + conv_kernel[offset][None, :] * extended[offset:offset + TOKENS]
    key_grad = key_sum.astype(jnp.bfloat16)
    key_input = jnp.dot(key_grad, w_key.T, preferred_element_type=jnp.float32)

    block_ids = route_ids.reshape(N_CTX, TOK_C * TOP).astype(jnp.int32)
    expert_hot = (block_ids[:, :, None] == jnp.arange(EXPERTS, dtype=jnp.int32)[None, None, :]).astype(jnp.int32)
    arrival = jnp.sum((jnp.cumsum(expert_hot, 1) - expert_hot) * expert_hot, 2).astype(jnp.int32)
    row_index = (jnp.arange(N_CTX, dtype=jnp.int32)[:, None] * CAP + arrival).astype(jnp.int32)
    route_count = TOKENS * TOP
    route_table = jnp.full((EXPERTS, N_CTX * CAP), route_count, jnp.int32)
    route_table = route_table.at[block_ids.reshape(-1), row_index.reshape(-1)].set(jnp.arange(route_count, dtype=jnp.int32))
    probs_padded = jnp.concatenate([route_probs.reshape(-1), jnp.zeros((1,), route_probs.dtype)])
    token_of = jnp.concatenate([jnp.arange(route_count, dtype=jnp.int32) // TOP, jnp.full((1,), TOKENS, jnp.int32)])
    grad_padded = jnp.concatenate([moe_grad, jnp.zeros((1, D), moe_grad.dtype)], 0)
    ff_dev = FF // SPLIT

    def one_expert(accumulated, expert_items):
        entries, up_blocks, down_blocks, gate_blocks, up_saved = expert_items
        tokens = token_of[entries]
        scaled = (probs_padded[entries][:, None] * grad_padded[tokens].astype(jnp.float32)).astype(jnp.bfloat16)
        hidden_grad = jnp.einsum("rd,qfd->qrf", scaled.astype(jnp.float32), down_blocks.astype(jnp.float32))
        gate_pre = gate_blocks.reshape(SPLIT, N_CTX * CAP, ff_dev).astype(jnp.float32)
        up_output = up_saved.reshape(SPLIT, N_CTX * CAP, ff_dev).astype(jnp.float32)
        gate_grad = (hidden_grad * up_output * silu_slope(gate_pre)).astype(jnp.bfloat16)
        up_grad = (hidden_grad * jax.nn.silu(gate_pre)).astype(jnp.bfloat16)
        partial_rows = jnp.einsum("qrf,qdf->qrd", up_grad.astype(jnp.float32), up_blocks.astype(jnp.float32)).astype(jnp.bfloat16)
        summed = jnp.sum(partial_rows.astype(jnp.float32), 0)
        accumulated = accumulated.at[tokens].add(summed, mode="drop")
        return accumulated, gate_grad.reshape(SPLIT, N_CTX, CAP, ff_dev)

    expert_items = (
        route_table,
        w_up.reshape(EXPERTS, SPLIT, D, ff_dev),
        w_down.reshape(EXPERTS, SPLIT, ff_dev, D),
        saved_gate.reshape(EXPERTS, SPLIT, N_CTX, CAP, ff_dev),
        saved_up.reshape(EXPERTS, SPLIT, N_CTX, CAP, ff_dev),
    )
    moe_input, gate_stack = lax.scan(one_expert, jnp.zeros((TOKENS, D), jnp.float32), expert_items)
    input_grad = moe_input + key_input
    return input_grad, gate_stack.reshape(EXPERTS * SPLIT, N_CTX, CAP, ff_dev)
```

```python
import jax
import jax.numpy as jnp
from jax import lax
from jax.sharding import Mesh
from jax.sharding import PartitionSpec as P

SPLIT = 4


def passed_along(value, axis, steps):
    count = lax.axis_size(axis)
    leading, last = (max(0, -steps), min(count, count - steps))
    return lax.ppermute(value, axis, [(source, source + steps) for source in range(leading, last)])


def silu_slope(values):
    logistic = jax.nn.sigmoid(values)
    return logistic * (1.0 + values * (1.0 - logistic))


def contract_last(first_operand, second_operand):
    return lax.dot_general(
        first_operand, second_operand, (((1,), (1,)), ((), ())), preferred_element_type=jnp.float32
    )


def local(
    route_ids,
    route_probs,
    moe_grad,
    saved_gate,
    saved_up,
    w_up,
    w_down,
    conv_grad,
    conv_pre,
    conv_kernel,
    w_key,
):
    ctx_count = lax.axis_size("ctx")
    groups = lax.axis_size("g")
    split = lax.axis_size("q")
    my_group = lax.axis_index("g")
    my_quarter = lax.axis_index("q")
    tok_rows, top_count = route_ids.shape
    features = moe_grad.shape[1]
    capacity = saved_gate.shape[2]
    slot_count = ctx_count * capacity
    expert_count = ctx_count * groups
    tap_count = conv_kernel.shape[0]
    grad_pre = conv_grad.astype(jnp.float32) * silu_slope(conv_pre.astype(jnp.float32))
    following = passed_along(grad_pre[: tap_count - 1], "ctx", -1)
    extended = jnp.concatenate([grad_pre, following], 0)
    key_sum = conv_kernel[0][None, :] * extended[0:tok_rows]
    for offset in range(1, tap_count):
        key_sum = key_sum + conv_kernel[offset][None, :] * extended[offset : offset + tok_rows]
    key_grad = key_sum.astype(jnp.bfloat16)
    key_input = contract_last(lax.all_gather(key_grad, ("g", "q"), axis=1, tiled=True), w_key)
    flat_ids = route_ids.reshape(-1)
    expert_hot = (flat_ids[:, None] == jnp.arange(expert_count, dtype=jnp.int32)[None, :]).astype(
        jnp.int32
    )
    earlier = jnp.cumsum(expert_hot, 0) - expert_hot
    arrival = jnp.sum(earlier * expert_hot, 1)
    expert_group = flat_ids % groups
    slot_index = flat_ids // groups * capacity + arrival
    own_slot = jnp.where(expert_group == my_group, slot_index, -1).reshape(tok_rows, top_count)
    own_hit = own_slot[:, :, None] == jnp.arange(slot_count, dtype=jnp.int32)[None, None, :]
    placement = jnp.sum(own_hit.astype(jnp.float32), 1).astype(jnp.bfloat16)
    slot_probs = jnp.sum(jnp.where(own_hit, route_probs[:, :, None], 0.0), (0, 1))
    chunk = features // split
    grad_chunk = lax.dynamic_slice_in_dim(moe_grad, my_quarter * chunk, chunk, axis=1)
    picked = lax.dot_general(
        placement, grad_chunk, (((0,), (0,)), ((), ())), preferred_element_type=jnp.float32
    )
    scaled_rows = (slot_probs[:, None] * picked).astype(jnp.bfloat16)
    got_rows = lax.all_to_all(scaled_rows, "ctx", split_axis=0, concat_axis=0, tiled=True)
    got_rows = lax.all_gather(got_rows, "q", axis=1, tiled=True)
    gate_pre = saved_gate.reshape(slot_count, -1).astype(jnp.float32)
    up_output = saved_up.reshape(slot_count, -1).astype(jnp.float32)
    hidden_grad = contract_last(got_rows, w_down[0])
    gate_grad = (hidden_grad * up_output * silu_slope(gate_pre)).astype(jnp.bfloat16)
    up_grad = (hidden_grad * jax.nn.silu(gate_pre)).astype(jnp.bfloat16)
    block = features // (groups * split)
    up_blocks = w_up[0].reshape(groups, split, block, -1)
    partial_rows = jnp.einsum(
        "sh,gqfh->qsgf", up_grad, up_blocks, preferred_element_type=jnp.float32
    ).astype(jnp.bfloat16)
    partial_rows = partial_rows.reshape(split * slot_count, groups * block)
    summed_rows = lax.psum_scatter(partial_rows, "q", scatter_dimension=0, tiled=True)
    came_back = lax.all_to_all(summed_rows, "ctx", split_axis=0, concat_axis=0, tiled=True)
    token_rows = jnp.dot(placement, came_back, preferred_element_type=jnp.float32)
    moe_share = lax.psum_scatter(token_rows, "g", scatter_dimension=1, tiled=True)
    input_grad = moe_share + key_input
    return (input_grad, gate_grad.reshape(saved_gate.shape))


def solution(mesh):
    ctx_count, exp_count = mesh.devices.shape
    split_mesh = Mesh(
        mesh.devices.reshape(ctx_count, exp_count // SPLIT, SPLIT), ("ctx", "g", "q")
    )
    exp = ("g", "q")
    return jax.shard_map(
        local,
        mesh=split_mesh,
        in_specs=(
            P("ctx", None),
            P("ctx", None),
            P("ctx", None),
            P(("ctx", *exp), None, None, None),
            P(("ctx", *exp), None, None, None),
            P(("ctx", *exp), None, None),
            P(("ctx", *exp), None, None),
            P("ctx", exp),
            P("ctx", exp),
            P(None, exp),
            P(exp, None),
        ),
        out_specs=(P("ctx", exp), P(("ctx", *exp), None, None, None)),
        check_vma=False,
    )
```

```python
import jax
import jax.numpy as jnp
from jax import lax
from jax.sharding import Mesh
from jax.sharding import PartitionSpec as P

SPLIT = 4
CORES = 2
CTX = ("z", "k")


def passed_along(value, axis, steps):
    count = lax.axis_size(axis)
    leading, last = (max(0, -steps), min(count, count - steps))
    return lax.ppermute(value, axis, [(source, source + steps) for source in range(leading, last)])


def across_ctx(rows):
    chips, cores = lax.axis_size("z"), lax.axis_size("k")
    blocks = rows.reshape(chips, cores, -1, rows.shape[-1])
    blocks = lax.all_to_all(blocks, "k", split_axis=1, concat_axis=1, tiled=True)
    blocks = lax.all_to_all(blocks, "z", split_axis=0, concat_axis=0, tiled=True)
    return blocks.reshape(rows.shape)


def silu_slope(values):
    logistic = jax.nn.sigmoid(values)
    return logistic * (1.0 + values * (1.0 - logistic))


def contract_last(first_operand, second_operand):
    return lax.dot_general(
        first_operand, second_operand, (((1,), (1,)), ((), ())), preferred_element_type=jnp.float32
    )


def local(
    route_ids,
    route_probs,
    moe_grad,
    saved_gate,
    saved_up,
    w_up,
    w_down,
    conv_grad,
    conv_pre,
    conv_kernel,
    w_key,
):
    ctx_count = lax.axis_size(CTX)
    groups = lax.axis_size("g")
    split = lax.axis_size("q")
    my_group = lax.axis_index("g")
    my_quarter = lax.axis_index("q")
    tok_rows, top_count = route_ids.shape
    features = moe_grad.shape[1]
    capacity = saved_gate.shape[2]
    slot_count = ctx_count * capacity
    expert_count = ctx_count * groups
    tap_count = conv_kernel.shape[0]
    grad_pre = conv_grad.astype(jnp.float32) * silu_slope(conv_pre.astype(jnp.float32))
    following = passed_along(grad_pre[: tap_count - 1], CTX, -1)
    extended = jnp.concatenate([grad_pre, following], 0)
    key_sum = conv_kernel[0][None, :] * extended[0:tok_rows]
    for offset in range(1, tap_count):
        key_sum = key_sum + conv_kernel[offset][None, :] * extended[offset : offset + tok_rows]
    key_grad = key_sum.astype(jnp.bfloat16)
    key_input = contract_last(lax.all_gather(key_grad, ("g", "q"), axis=1, tiled=True), w_key)
    flat_ids = route_ids.reshape(-1)
    expert_hot = (flat_ids[:, None] == jnp.arange(expert_count, dtype=jnp.int32)[None, :]).astype(
        jnp.int32
    )
    earlier = jnp.cumsum(expert_hot, 0) - expert_hot
    arrival = jnp.sum(earlier * expert_hot, 1)
    expert_group = flat_ids % groups
    slot_index = flat_ids // groups * capacity + arrival
    own_slot = jnp.where(expert_group == my_group, slot_index, -1).reshape(tok_rows, top_count)
    own_hit = own_slot[:, :, None] == jnp.arange(slot_count, dtype=jnp.int32)[None, None, :]
    placement = jnp.sum(own_hit.astype(jnp.float32), 1).astype(jnp.bfloat16)
    slot_probs = jnp.sum(jnp.where(own_hit, route_probs[:, :, None], 0.0), (0, 1))
    chunk = features // split
    grad_chunk = lax.dynamic_slice_in_dim(moe_grad, my_quarter * chunk, chunk, axis=1)
    picked = lax.dot_general(
        placement, grad_chunk, (((0,), (0,)), ((), ())), preferred_element_type=jnp.float32
    )
    scaled_rows = (slot_probs[:, None] * picked).astype(jnp.bfloat16)
    got_rows = across_ctx(scaled_rows)
    got_rows = lax.all_gather(got_rows, "q", axis=1, tiled=True)
    gate_pre = saved_gate.reshape(slot_count, -1).astype(jnp.float32)
    up_output = saved_up.reshape(slot_count, -1).astype(jnp.float32)
    hidden_grad = contract_last(got_rows, w_down[0])
    gate_grad = (hidden_grad * up_output * silu_slope(gate_pre)).astype(jnp.bfloat16)
    up_grad = (hidden_grad * jax.nn.silu(gate_pre)).astype(jnp.bfloat16)
    block = features // (groups * split)
    up_blocks = w_up[0].reshape(groups, split, block, -1)
    partial_rows = jnp.einsum(
        "sh,gqfh->qsgf", up_grad, up_blocks, preferred_element_type=jnp.float32
    ).astype(jnp.bfloat16)
    partial_rows = partial_rows.reshape(split * slot_count, groups * block)
    summed_rows = lax.psum_scatter(partial_rows, "q", scatter_dimension=0, tiled=True)
    came_back = across_ctx(summed_rows)
    token_rows = jnp.dot(placement, came_back, preferred_element_type=jnp.float32)
    moe_share = lax.psum_scatter(token_rows, "g", scatter_dimension=1, tiled=True)
    input_grad = moe_share + key_input
    return (input_grad, gate_grad.reshape(saved_gate.shape))


def solution(mesh):
    ctx_count, exp_count = mesh.devices.shape
    split_mesh = Mesh(
        mesh.devices.reshape(ctx_count // CORES, CORES, exp_count // SPLIT, SPLIT),
        (*CTX, "g", "q"),
    )
    exp = ("g", "q")
    return jax.shard_map(
        local,
        mesh=split_mesh,
        in_specs=(
            P(CTX, None),
            P(CTX, None),
            P(CTX, None),
            P((*CTX, *exp), None, None, None),
            P((*CTX, *exp), None, None, None),
            P((*CTX, *exp), None, None),
            P((*CTX, *exp), None, None),
            P(CTX, exp),
            P(CTX, exp),
            P(None, exp),
            P(exp, None),
        ),
        out_specs=(P(CTX, exp), P((*CTX, *exp), None, None, None)),
        check_vma=False,
    )
```

```python
import jax
import jax.numpy as jnp
from jax import lax
from jax.sharding import Mesh
from jax.sharding import PartitionSpec as P

SPLIT = 4
CORES = 2
CTX = ("z", "k")


def passed_along(value, axis, steps):
    count = lax.axis_size(axis)
    leading, last = (max(0, -steps), min(count, count - steps))
    return lax.ppermute(value, axis, [(source, source + steps) for source in range(leading, last)])


def across_ctx(rows):
    chips, cores = lax.axis_size("z"), lax.axis_size("k")
    blocks = rows.reshape(chips, cores, -1, rows.shape[-1])
    blocks = lax.all_to_all(blocks, "k", split_axis=1, concat_axis=1, tiled=True)
    blocks = lax.all_to_all(blocks, "z", split_axis=0, concat_axis=0, tiled=True)
    return blocks.reshape(rows.shape)


def silu_slope(values):
    logistic = jax.nn.sigmoid(values)
    return logistic * (1.0 + values * (1.0 - logistic))


def contract_last(first_operand, second_operand):
    return lax.dot_general(
        first_operand, second_operand, (((1,), (1,)), ((), ())), preferred_element_type=jnp.float32
    )


def local(
    route_ids,
    route_probs,
    moe_grad,
    saved_gate,
    saved_up,
    w_up,
    w_down,
    conv_grad,
    conv_pre,
    conv_kernel,
    w_key,
):
    ctx_count = lax.axis_size(CTX)
    groups = lax.axis_size("g")
    split = lax.axis_size("q")
    my_group = lax.axis_index("g")
    my_quarter = lax.axis_index("q")
    tok_rows, top_count = route_ids.shape
    features = moe_grad.shape[1]
    capacity = saved_gate.shape[2]
    slot_count = ctx_count * capacity
    expert_count = ctx_count * groups
    tap_count = conv_kernel.shape[0]
    grad_pre = conv_grad.astype(jnp.float32) * silu_slope(conv_pre.astype(jnp.float32))
    following = passed_along(grad_pre[: tap_count - 1], CTX, -1)
    extended = jnp.concatenate([grad_pre, following], 0)
    key_sum = conv_kernel[0][None, :] * extended[0:tok_rows]
    for offset in range(1, tap_count):
        key_sum = key_sum + conv_kernel[offset][None, :] * extended[offset : offset + tok_rows]
    key_grad = key_sum.astype(jnp.bfloat16)
    flat_ids = route_ids.reshape(-1)
    expert_hot = (flat_ids[:, None] == jnp.arange(expert_count, dtype=jnp.int32)[None, :]).astype(
        jnp.int32
    )
    earlier = jnp.cumsum(expert_hot, 0) - expert_hot
    arrival = jnp.sum(earlier * expert_hot, 1)
    expert_group = flat_ids % groups
    slot_index = flat_ids // groups * capacity + arrival
    own_slot = jnp.where(expert_group == my_group, slot_index, -1).reshape(tok_rows, top_count)
    own_hit = own_slot[:, :, None] == jnp.arange(slot_count, dtype=jnp.int32)[None, None, :]
    placement = jnp.sum(own_hit.astype(jnp.float32), 1).astype(jnp.bfloat16)
    slot_probs = jnp.sum(jnp.where(own_hit, route_probs[:, :, None], 0.0), (0, 1))
    chunk = features // split
    grad_chunk = lax.dynamic_slice_in_dim(moe_grad, my_quarter * chunk, chunk, axis=1)
    picked = lax.dot_general(
        placement, grad_chunk, (((0,), (0,)), ((), ())), preferred_element_type=jnp.float32
    )
    scaled_rows = (slot_probs[:, None] * picked).astype(jnp.bfloat16)
    key_grad, scaled_rows = lax.optimization_barrier((key_grad, scaled_rows))
    key_all = lax.all_gather(key_grad, ("g", "q"), axis=1, tiled=True)
    got_rows = across_ctx(scaled_rows)
    key_all, got_rows = lax.optimization_barrier((key_all, got_rows))
    key_input = contract_last(key_all, w_key)
    got_rows = lax.all_gather(got_rows, "q", axis=1, tiled=True)
    gate_pre = saved_gate.reshape(slot_count, -1).astype(jnp.float32)
    up_output = saved_up.reshape(slot_count, -1).astype(jnp.float32)
    hidden_grad = contract_last(got_rows, w_down[0])
    gate_grad = (hidden_grad * up_output * silu_slope(gate_pre)).astype(jnp.bfloat16)
    up_grad = (hidden_grad * jax.nn.silu(gate_pre)).astype(jnp.bfloat16)
    block = features // (groups * split)
    up_blocks = w_up[0].reshape(groups, split, block, -1).transpose(1, 0, 2, 3)
    partial_rows = contract_last(up_grad, up_blocks.reshape(features, -1)).astype(jnp.bfloat16)
    summed_rows = lax.psum_scatter(partial_rows, "q", scatter_dimension=1, tiled=True)
    came_back = across_ctx(summed_rows)
    token_rows = jnp.dot(placement, came_back, preferred_element_type=jnp.float32)
    moe_share = lax.psum_scatter(token_rows, "g", scatter_dimension=1, tiled=True)
    input_grad = moe_share + key_input
    return (input_grad, gate_grad.reshape(saved_gate.shape))


def solution(mesh):
    ctx_count, exp_count = mesh.devices.shape
    split_mesh = Mesh(
        mesh.devices.reshape(ctx_count // CORES, CORES, exp_count // SPLIT, SPLIT),
        (*CTX, "g", "q"),
    )
    exp = ("g", "q")
    return jax.shard_map(
        local,
        mesh=split_mesh,
        in_specs=(
            P(CTX, None),
            P(CTX, None),
            P(CTX, None),
            P((*CTX, *exp), None, None, None),
            P((*CTX, *exp), None, None, None),
            P((*CTX, *exp), None, None),
            P((*CTX, *exp), None, None),
            P(CTX, exp),
            P(CTX, exp),
            P(None, exp),
            P(exp, None),
        ),
        out_specs=(P(CTX, exp), P((*CTX, *exp), None, None, None)),
        check_vma=False,
    )
```

```python
import jax
import jax.numpy as jnp
from jax import lax
from jax.sharding import Mesh
from jax.sharding import PartitionSpec as P

SPLIT = 4
CORES = 2
CTX = ("z", "k")


def passed_along(value, axis, steps):
    count = lax.axis_size(axis)
    leading, last = (max(0, -steps), min(count, count - steps))
    return lax.ppermute(value, axis, [(source, source + steps) for source in range(leading, last)])


def across_ctx(rows):
    chips, cores = lax.axis_size("z"), lax.axis_size("k")
    blocks = rows.reshape(chips, cores, -1, rows.shape[-1])
    blocks = lax.all_to_all(blocks, "k", split_axis=1, concat_axis=1, tiled=True)
    blocks = lax.all_to_all(blocks, "z", split_axis=0, concat_axis=0, tiled=True)
    return blocks.reshape(rows.shape)


def silu_slope(values):
    logistic = jax.nn.sigmoid(values)
    return logistic * (1.0 + values * (1.0 - logistic))


def contract_last(first_operand, second_operand):
    return lax.dot_general(
        first_operand, second_operand, (((1,), (1,)), ((), ())), preferred_element_type=jnp.float32
    )


def local(
    route_ids,
    route_probs,
    moe_grad,
    saved_gate,
    saved_up,
    w_up,
    w_down,
    conv_grad,
    conv_pre,
    conv_kernel,
    w_key,
):
    ctx_count = lax.axis_size(CTX)
    groups = lax.axis_size("g")
    split = lax.axis_size("q")
    my_group = lax.axis_index("g")
    my_quarter = lax.axis_index("q")
    tok_rows, top_count = route_ids.shape
    features = moe_grad.shape[1]
    capacity = saved_gate.shape[2]
    slot_count = ctx_count * capacity
    expert_count = ctx_count * groups
    tap_count = conv_kernel.shape[0]
    grad_pre = conv_grad.astype(jnp.float32) * silu_slope(conv_pre.astype(jnp.float32))
    following = passed_along(grad_pre[: tap_count - 1], CTX, -1)
    extended = jnp.concatenate([grad_pre, following], 0)
    key_sum = conv_kernel[0][None, :] * extended[0:tok_rows]
    for offset in range(1, tap_count):
        key_sum = key_sum + conv_kernel[offset][None, :] * extended[offset : offset + tok_rows]
    key_grad = key_sum.astype(jnp.bfloat16)
    flat_ids = route_ids.reshape(-1)
    expert_hot = (flat_ids[:, None] == jnp.arange(expert_count, dtype=jnp.int32)[None, :]).astype(
        jnp.int32
    )
    earlier = jnp.cumsum(expert_hot, 0) - expert_hot
    arrival = jnp.sum(earlier * expert_hot, 1)
    expert_group = flat_ids % groups
    slot_index = flat_ids // groups * capacity + arrival
    own_slot = jnp.where(expert_group == my_group, slot_index, -1).reshape(tok_rows, top_count)
    own_hit = own_slot[:, :, None] == jnp.arange(slot_count, dtype=jnp.int32)[None, None, :]
    placement = jnp.sum(own_hit.astype(jnp.float32), 1).astype(jnp.bfloat16)
    slot_probs = jnp.sum(jnp.where(own_hit, route_probs[:, :, None], 0.0), (0, 1))
    chunk = features // split
    grad_chunk = lax.dynamic_slice_in_dim(moe_grad, my_quarter * chunk, chunk, axis=1)
    picked = lax.dot_general(
        placement, grad_chunk, (((0,), (0,)), ((), ())), preferred_element_type=jnp.float32
    )
    scaled_rows = (slot_probs[:, None] * picked).astype(jnp.bfloat16)
    key_grad, scaled_rows = lax.optimization_barrier((key_grad, scaled_rows))
    key_all = lax.all_gather(key_grad, ("g", "q"), axis=1, tiled=True)
    got_rows = across_ctx(scaled_rows)
    key_all, got_rows = lax.optimization_barrier((key_all, got_rows))
    key_input = contract_last(key_all, w_key)
    got_rows = lax.all_to_all(
        jnp.broadcast_to(got_rows[None], (split, *got_rows.shape)), "q", 0, 0, tiled=True
    )
    gate_pre = saved_gate.reshape(slot_count, -1).astype(jnp.float32)
    up_output = saved_up.reshape(slot_count, -1).astype(jnp.float32)
    hidden_grad = jnp.einsum(
        "qsf,hqf->sh",
        got_rows,
        w_down[0].reshape(-1, split, chunk),
        preferred_element_type=jnp.float32,
    )
    gate_grad = (hidden_grad * up_output * silu_slope(gate_pre)).astype(jnp.bfloat16)
    up_grad = (hidden_grad * jax.nn.silu(gate_pre)).astype(jnp.bfloat16)
    block = features // (groups * split)
    up_blocks = w_up[0].reshape(groups, split, block, -1).transpose(1, 0, 2, 3)
    partial_rows = contract_last(up_grad, up_blocks.reshape(features, -1)).astype(jnp.bfloat16)
    partial_rows = partial_rows.reshape(slot_count, split, -1)
    partial_rows = lax.all_to_all(partial_rows, "q", 1, 1, tiled=True)
    summed_rows = jnp.sum(partial_rows.astype(jnp.float32), 1).astype(jnp.bfloat16)
    came_back = across_ctx(summed_rows)
    token_rows = jnp.dot(placement, came_back, preferred_element_type=jnp.float32)
    moe_share = lax.psum_scatter(token_rows, "g", scatter_dimension=1, tiled=True)
    input_grad = moe_share + key_input
    return (input_grad, gate_grad.reshape(saved_gate.shape))


def solution(mesh):
    ctx_count, exp_count = mesh.devices.shape
    split_mesh = Mesh(
        mesh.devices.reshape(ctx_count // CORES, CORES, exp_count // SPLIT, SPLIT),
        (*CTX, "g", "q"),
    )
    exp = ("g", "q")
    return jax.shard_map(
        local,
        mesh=split_mesh,
        in_specs=(
            P(CTX, None),
            P(CTX, None),
            P(CTX, None),
            P((*CTX, *exp), None, None, None),
            P((*CTX, *exp), None, None, None),
            P((*CTX, *exp), None, None),
            P((*CTX, *exp), None, None),
            P(CTX, exp),
            P(CTX, exp),
            P(None, exp),
            P(exp, None),
        ),
        out_specs=(P(CTX, exp), P((*CTX, *exp), None, None, None)),
        check_vma=False,
    )
```

```python
import jax
import jax.numpy as jnp
from jax import lax
from jax.sharding import Mesh
from jax.sharding import PartitionSpec as P

SPLIT = 4
CORES = 2
CTX = ("z", "k")


def passed_along(value, axis, steps):
    count = lax.axis_size(axis)
    leading, last = (max(0, -steps), min(count, count - steps))
    return lax.ppermute(value, axis, [(source, source + steps) for source in range(leading, last)])


def across_ctx(rows):
    chips, cores = lax.axis_size("z"), lax.axis_size("k")
    blocks = rows.reshape(chips, cores, -1, rows.shape[-1])
    blocks = lax.all_to_all(blocks, "k", split_axis=1, concat_axis=1, tiled=True)
    blocks = lax.all_to_all(blocks, "z", split_axis=0, concat_axis=0, tiled=True)
    return blocks.reshape(rows.shape)


def silu_slope(values):
    logistic = jax.nn.sigmoid(values)
    return logistic * (1.0 + values * (1.0 - logistic))


def contract_last(first_operand, second_operand):
    return lax.dot_general(
        first_operand, second_operand, (((1,), (1,)), ((), ())), preferred_element_type=jnp.float32
    )


def local(
    route_ids,
    route_probs,
    moe_grad,
    saved_gate,
    saved_up,
    w_up,
    w_down,
    conv_grad,
    conv_pre,
    conv_kernel,
    w_key,
):
    ctx_count = lax.axis_size(CTX)
    groups = lax.axis_size("g")
    split = lax.axis_size("q")
    my_group = lax.axis_index("g")
    my_quarter = lax.axis_index("q")
    tok_rows, top_count = route_ids.shape
    features = moe_grad.shape[1]
    capacity = saved_gate.shape[2]
    slot_count = ctx_count * capacity
    expert_count = ctx_count * groups
    tap_count = conv_kernel.shape[0]
    grad_pre = conv_grad.astype(jnp.float32) * silu_slope(conv_pre.astype(jnp.float32))
    following = passed_along(grad_pre[: tap_count - 1], CTX, -1)
    extended = jnp.concatenate([grad_pre, following], 0)
    key_sum = conv_kernel[0][None, :] * extended[0:tok_rows]
    for offset in range(1, tap_count):
        key_sum = key_sum + conv_kernel[offset][None, :] * extended[offset : offset + tok_rows]
    key_grad = key_sum.astype(jnp.bfloat16)
    flat_ids = route_ids.reshape(-1)
    expert_hot = (flat_ids[:, None] == jnp.arange(expert_count, dtype=jnp.int32)[None, :]).astype(
        jnp.int32
    )
    earlier = jnp.cumsum(expert_hot, 0) - expert_hot
    arrival = jnp.sum(earlier * expert_hot, 1)
    expert_group = flat_ids % groups
    slot_index = flat_ids // groups * capacity + arrival
    own_slot = jnp.where(expert_group == my_group, slot_index, -1).reshape(tok_rows, top_count)
    own_hit = own_slot[:, :, None] == jnp.arange(slot_count, dtype=jnp.int32)[None, None, :]
    placement = jnp.sum(own_hit.astype(jnp.float32), 1).astype(jnp.bfloat16)
    slot_probs = jnp.sum(jnp.where(own_hit, route_probs[:, :, None], 0.0), (0, 1))
    chunk = features // split
    grad_chunk = lax.dynamic_slice_in_dim(moe_grad, my_quarter * chunk, chunk, axis=1)
    picked = lax.dot_general(
        placement, grad_chunk, (((0,), (0,)), ((), ())), preferred_element_type=jnp.float32
    )
    scaled_rows = (slot_probs[:, None] * picked).astype(jnp.bfloat16)
    key_grad, scaled_rows = lax.optimization_barrier((key_grad, scaled_rows))
    key_all = lax.all_gather(key_grad, "q", axis=1, tiled=True)
    key_all = lax.all_gather(key_all, "g", axis=1, tiled=True)
    got_rows = across_ctx(scaled_rows)
    key_all, got_rows = lax.optimization_barrier((key_all, got_rows))
    key_input = contract_last(key_all, w_key)
    got_rows = lax.all_to_all(
        jnp.broadcast_to(got_rows[None], (split, *got_rows.shape)), "q", 0, 0, tiled=True
    )
    gate_pre = saved_gate.reshape(slot_count, -1).astype(jnp.float32)
    up_output = saved_up.reshape(slot_count, -1).astype(jnp.float32)
    hidden_grad = jnp.einsum(
        "qsf,hqf->sh",
        got_rows,
        w_down[0].reshape(-1, split, chunk),
        preferred_element_type=jnp.float32,
    )
    gate_grad = (hidden_grad * up_output * silu_slope(gate_pre)).astype(jnp.bfloat16)
    up_grad = (hidden_grad * jax.nn.silu(gate_pre)).astype(jnp.bfloat16)
    block = features // (groups * split)
    up_blocks = w_up[0].reshape(groups, split, block, -1).transpose(1, 0, 2, 3)
    partial_rows = contract_last(up_grad, up_blocks.reshape(features, -1)).astype(jnp.bfloat16)
    partial_rows = partial_rows.reshape(slot_count, split, -1)
    partial_rows = lax.all_to_all(partial_rows, "q", 1, 1, tiled=True)
    summed_rows = jnp.sum(partial_rows.astype(jnp.float32), 1).astype(jnp.bfloat16)
    came_back = across_ctx(summed_rows)
    token_rows = jnp.dot(placement, came_back, preferred_element_type=jnp.float32)
    token_rows = lax.all_to_all(token_rows.reshape(tok_rows, groups, -1), "g", 1, 1, tiled=True)
    moe_share = jnp.sum(token_rows, 1)
    input_grad = moe_share + key_input
    return (input_grad, gate_grad.reshape(saved_gate.shape))


def solution(mesh):
    ctx_count, exp_count = mesh.devices.shape
    split_mesh = Mesh(
        mesh.devices.reshape(ctx_count // CORES, CORES, exp_count // SPLIT, SPLIT),
        (*CTX, "g", "q"),
    )
    exp = ("g", "q")
    return jax.shard_map(
        local,
        mesh=split_mesh,
        in_specs=(
            P(CTX, None),
            P(CTX, None),
            P(CTX, None),
            P((*CTX, *exp), None, None, None),
            P((*CTX, *exp), None, None, None),
            P((*CTX, *exp), None, None),
            P((*CTX, *exp), None, None),
            P(CTX, exp),
            P(CTX, exp),
            P(None, exp),
            P(exp, None),
        ),
        out_specs=(P(CTX, exp), P((*CTX, *exp), None, None, None)),
        check_vma=False,
    )
```

```python
import jax
import jax.numpy as jnp
from jax import lax
from jax.sharding import Mesh
from jax.sharding import PartitionSpec as P

SPLIT = 4
CORES = 2
CTX = ("z", "k")


def passed_along(value, axis, steps):
    count = lax.axis_size(axis)
    leading, last = (max(0, -steps), min(count, count - steps))
    return lax.ppermute(value, axis, [(source, source + steps) for source in range(leading, last)])


def silu_slope(values):
    logistic = jax.nn.sigmoid(values)
    return logistic * (1.0 + values * (1.0 - logistic))


def contract_last(first_operand, second_operand):
    return lax.dot_general(
        first_operand, second_operand, (((1,), (1,)), ((), ())), preferred_element_type=jnp.float32
    )


def local(
    route_ids,
    route_probs,
    moe_grad,
    saved_gate,
    saved_up,
    w_up,
    w_down,
    conv_grad,
    conv_pre,
    conv_kernel,
    w_key,
):
    ctx_count = lax.axis_size(CTX)
    groups = lax.axis_size("g")
    split = lax.axis_size("q")
    my_group = lax.axis_index("g")
    my_quarter = lax.axis_index("q")
    tok_rows, top_count = route_ids.shape
    features = moe_grad.shape[1]
    capacity = saved_gate.shape[2]
    slot_count = ctx_count * capacity
    expert_count = ctx_count * groups
    tap_count = conv_kernel.shape[0]
    grad_pre = conv_grad.astype(jnp.float32) * silu_slope(conv_pre.astype(jnp.float32))
    following = passed_along(grad_pre[: tap_count - 1], CTX, -1)
    extended = jnp.concatenate([grad_pre, following], 0)
    key_sum = conv_kernel[0][None, :] * extended[0:tok_rows]
    for offset in range(1, tap_count):
        key_sum = key_sum + conv_kernel[offset][None, :] * extended[offset : offset + tok_rows]
    key_grad = key_sum.astype(jnp.bfloat16)
    flat_ids = route_ids.reshape(-1)
    expert_hot = (flat_ids[:, None] == jnp.arange(expert_count, dtype=jnp.int32)[None, :]).astype(
        jnp.int32
    )
    earlier = jnp.cumsum(expert_hot, 0) - expert_hot
    arrival = jnp.sum(earlier * expert_hot, 1)
    expert_group = flat_ids % groups
    slot_index = flat_ids // groups * capacity + arrival
    own_slot = jnp.where(expert_group == my_group, slot_index, -1).reshape(tok_rows, top_count)
    own_hit = own_slot[:, :, None] == jnp.arange(slot_count, dtype=jnp.int32)[None, None, :]
    placement = jnp.sum(own_hit.astype(jnp.float32), 1).astype(jnp.bfloat16)
    slot_probs = jnp.sum(jnp.where(own_hit, route_probs[:, :, None], 0.0), (0, 1))
    chunk = features // split
    grad_chunk = lax.dynamic_slice_in_dim(moe_grad, my_quarter * chunk, chunk, axis=1)
    picked = lax.dot_general(
        placement, grad_chunk, (((0,), (0,)), ((), ())), preferred_element_type=jnp.float32
    )
    scaled_rows = (slot_probs[:, None] * picked).astype(jnp.bfloat16)
    key_grad, scaled_rows = lax.optimization_barrier((key_grad, scaled_rows))
    key_all = lax.all_gather(key_grad, "q", axis=1, tiled=True)
    key_all = lax.all_gather(key_all, "g", axis=1, tiled=True)
    chips, cores = lax.axis_size("z"), lax.axis_size("k")
    got_rows = scaled_rows.reshape(chips, cores, capacity, chunk)
    got_rows = lax.all_to_all(got_rows, "z", 0, 0, tiled=True).transpose(1, 0, 2, 3)
    key_all, got_rows = lax.optimization_barrier((key_all, got_rows))
    key_input = contract_last(key_all, w_key)
    got_rows = jnp.broadcast_to(got_rows[:, None], (cores, split, chips, capacity, chunk))
    got_rows = got_rows.reshape(cores * split, chips, capacity, chunk)
    got_rows = lax.all_to_all(got_rows, ("k", "q"), 0, 0, tiled=True)
    got_rows = got_rows.reshape(cores, split, chips, capacity, chunk)
    gate_pre = saved_gate.reshape(slot_count, -1).astype(jnp.float32)
    up_output = saved_up.reshape(slot_count, -1).astype(jnp.float32)
    hidden_grad = jnp.einsum(
        "kqzsf,hqf->zksh",
        got_rows,
        w_down[0].reshape(-1, split, chunk),
        preferred_element_type=jnp.float32,
    ).reshape(slot_count, -1)
    gate_grad = (hidden_grad * up_output * silu_slope(gate_pre)).astype(jnp.bfloat16)
    up_grad = (hidden_grad * jax.nn.silu(gate_pre)).astype(jnp.bfloat16)
    block = features // (groups * split)
    up_blocks = w_up[0].reshape(groups, split, block, -1).transpose(1, 0, 2, 3)
    partial_rows = contract_last(up_grad, up_blocks.reshape(features, -1)).astype(jnp.bfloat16)
    partial_rows = partial_rows.reshape(chips, cores, capacity, split, chunk)
    partial_rows = partial_rows.transpose(1, 3, 0, 2, 4).reshape(cores * split, chips, capacity, chunk)
    partial_rows = lax.all_to_all(partial_rows, ("k", "q"), 0, 0, tiled=True)
    partial_rows = partial_rows.reshape(cores, split, chips, capacity, chunk)
    summed_rows = jnp.sum(partial_rows.astype(jnp.float32), 1).astype(jnp.bfloat16)
    summed_rows = summed_rows.transpose(1, 0, 2, 3)
    came_back = lax.all_to_all(summed_rows, "z", 0, 0, tiled=True).reshape(slot_count, chunk)
    token_rows = jnp.dot(placement, came_back, preferred_element_type=jnp.float32)
    token_rows = lax.all_to_all(token_rows.reshape(tok_rows, groups, -1), "g", 1, 1, tiled=True)
    moe_share = jnp.sum(token_rows, 1)
    input_grad = moe_share + key_input
    return (input_grad, gate_grad.reshape(saved_gate.shape))


def solution(mesh):
    ctx_count, exp_count = mesh.devices.shape
    split_mesh = Mesh(
        mesh.devices.reshape(ctx_count // CORES, CORES, exp_count // SPLIT, SPLIT),
        (*CTX, "g", "q"),
    )
    exp = ("g", "q")
    return jax.shard_map(
        local,
        mesh=split_mesh,
        in_specs=(
            P(CTX, None),
            P(CTX, None),
            P(CTX, None),
            P((*CTX, *exp), None, None, None),
            P((*CTX, *exp), None, None, None),
            P((*CTX, *exp), None, None),
            P((*CTX, *exp), None, None),
            P(CTX, exp),
            P(CTX, exp),
            P(None, exp),
            P(exp, None),
        ),
        out_specs=(P(CTX, exp), P((*CTX, *exp), None, None, None)),
        check_vma=False,
    )
```

```python
import jax
import jax.numpy as jnp
from jax import lax
from jax.sharding import Mesh
from jax.sharding import PartitionSpec as P

SPLIT = 4
CORES = 2
CTX = ("z", "k")


def passed_along(value, axis, steps):
    count = lax.axis_size(axis)
    leading, last = (max(0, -steps), min(count, count - steps))
    return lax.ppermute(value, axis, [(source, source + steps) for source in range(leading, last)])


def across_ctx(rows):
    chips, cores = lax.axis_size("z"), lax.axis_size("k")
    blocks = rows.reshape(chips, cores, -1, rows.shape[-1])
    blocks = lax.all_to_all(blocks, "k", split_axis=1, concat_axis=1, tiled=True)
    blocks = lax.all_to_all(blocks, "z", split_axis=0, concat_axis=0, tiled=True)
    return blocks.reshape(rows.shape)


def around(value, steps):
    count = lax.axis_size("q")
    return lax.ppermute(value, "q", [(source, (source + steps) % count) for source in range(count)])


def silu_slope(values):
    logistic = jax.nn.sigmoid(values)
    return logistic * (1.0 + values * (1.0 - logistic))


def contract_last(first_operand, second_operand):
    return lax.dot_general(
        first_operand, second_operand, (((1,), (1,)), ((), ())), preferred_element_type=jnp.float32
    )


def local(
    route_ids,
    route_probs,
    moe_grad,
    saved_gate,
    saved_up,
    w_up,
    w_down,
    conv_grad,
    conv_pre,
    conv_kernel,
    w_key,
):
    ctx_count = lax.axis_size(CTX)
    groups = lax.axis_size("g")
    split = lax.axis_size("q")
    my_group = lax.axis_index("g")
    my_quarter = lax.axis_index("q")
    tok_rows, top_count = route_ids.shape
    features = moe_grad.shape[1]
    capacity = saved_gate.shape[2]
    slot_count = ctx_count * capacity
    expert_count = ctx_count * groups
    tap_count = conv_kernel.shape[0]
    grad_pre = conv_grad.astype(jnp.float32) * silu_slope(conv_pre.astype(jnp.float32))
    following = passed_along(grad_pre[: tap_count - 1], CTX, -1)
    extended = jnp.concatenate([grad_pre, following], 0)
    key_sum = conv_kernel[0][None, :] * extended[0:tok_rows]
    for offset in range(1, tap_count):
        key_sum = key_sum + conv_kernel[offset][None, :] * extended[offset : offset + tok_rows]
    key_grad = key_sum.astype(jnp.bfloat16)
    flat_ids = route_ids.reshape(-1)
    expert_hot = (flat_ids[:, None] == jnp.arange(expert_count, dtype=jnp.int32)[None, :]).astype(
        jnp.int32
    )
    earlier = jnp.cumsum(expert_hot, 0) - expert_hot
    arrival = jnp.sum(earlier * expert_hot, 1)
    expert_group = flat_ids % groups
    slot_index = flat_ids // groups * capacity + arrival
    own_slot = jnp.where(expert_group == my_group, slot_index, -1).reshape(tok_rows, top_count)
    own_hit = own_slot[:, :, None] == jnp.arange(slot_count, dtype=jnp.int32)[None, None, :]
    placement = jnp.sum(own_hit.astype(jnp.float32), 1).astype(jnp.bfloat16)
    slot_probs = jnp.sum(jnp.where(own_hit, route_probs[:, :, None], 0.0), (0, 1))
    chunk = features // split
    grad_chunk = lax.dynamic_slice_in_dim(moe_grad, my_quarter * chunk, chunk, axis=1)
    picked = lax.dot_general(
        placement, grad_chunk, (((0,), (0,)), ((), ())), preferred_element_type=jnp.float32
    )
    scaled_rows = (slot_probs[:, None] * picked).astype(jnp.bfloat16)
    key_grad, scaled_rows = lax.optimization_barrier((key_grad, scaled_rows))
    key_all = lax.all_gather(key_grad, "q", axis=1, tiled=True)
    key_all = lax.all_gather(key_all, "g", axis=1, tiled=True)
    hidden = w_down.shape[1]
    block = features // (groups * split)
    down_own = w_down[0].reshape(hidden, split, chunk)
    up_own = w_up[0].reshape(groups, split, block, hidden)

    def down_slice(index):
        return lax.dynamic_index_in_dim(down_own, index, 1, keepdims=False)

    def up_slice(index):
        return lax.dynamic_index_in_dim(up_own, index, 1, keepdims=False).reshape(chunk, hidden)

    down_got = [down_slice(my_quarter)]
    up_got = [up_slice(my_quarter)]
    for shift in range(1, split):
        down_got.append(around(down_slice((my_quarter + shift) % split), shift))
        up_got.append(around(up_slice((my_quarter + shift) % split), shift))
    got_rows = across_ctx(scaled_rows)
    key_all, got_rows = lax.optimization_barrier((key_all, got_rows))
    key_input = contract_last(key_all, w_key)
    gate_pre = saved_gate.reshape(slot_count, -1).astype(jnp.float32)
    up_output = saved_up.reshape(slot_count, -1).astype(jnp.float32)
    hidden_grad = contract_last(got_rows, down_got[0])
    for shift in range(1, split):
        share = contract_last(got_rows, down_got[shift]).astype(jnp.bfloat16)
        hidden_grad = hidden_grad + around(share, -shift).astype(jnp.float32)
    gate_grad = (hidden_grad * up_output * silu_slope(gate_pre)).astype(jnp.bfloat16)
    up_grad = (hidden_grad * jax.nn.silu(gate_pre)).astype(jnp.bfloat16)
    summed_rows = contract_last(up_grad, up_got[0])
    for shift in range(1, split):
        summed_rows = summed_rows + contract_last(around(up_grad, shift), up_got[shift])
    summed_rows = summed_rows.astype(jnp.bfloat16)
    came_back = across_ctx(summed_rows)
    token_rows = jnp.dot(placement, came_back, preferred_element_type=jnp.float32)
    token_rows = lax.all_to_all(token_rows.reshape(tok_rows, groups, -1), "g", 1, 1, tiled=True)
    moe_share = jnp.sum(token_rows, 1)
    input_grad = moe_share + key_input
    return (input_grad, gate_grad.reshape(saved_gate.shape))


def solution(mesh):
    ctx_count, exp_count = mesh.devices.shape
    split_mesh = Mesh(
        mesh.devices.reshape(ctx_count // CORES, CORES, exp_count // SPLIT, SPLIT),
        (*CTX, "g", "q"),
    )
    exp = ("g", "q")
    return jax.shard_map(
        local,
        mesh=split_mesh,
        in_specs=(
            P(CTX, None),
            P(CTX, None),
            P(CTX, None),
            P((*CTX, *exp), None, None, None),
            P((*CTX, *exp), None, None, None),
            P((*CTX, *exp), None, None),
            P((*CTX, *exp), None, None),
            P(CTX, exp),
            P(CTX, exp),
            P(None, exp),
            P(exp, None),
        ),
        out_specs=(P(CTX, exp), P((*CTX, *exp), None, None, None)),
        check_vma=False,
    )
```

```python
import jax
import jax.numpy as jnp
from jax import lax
from jax.sharding import Mesh
from jax.sharding import PartitionSpec as P

SPLIT = 4
CORES = 2
CTX = ("z", "k")


def passed_along(value, axis, steps):
    count = lax.axis_size(axis)
    leading, last = (max(0, -steps), min(count, count - steps))
    return lax.ppermute(value, axis, [(source, source + steps) for source in range(leading, last)])


def across_ctx(rows):
    chips, cores = lax.axis_size("z"), lax.axis_size("k")
    blocks = rows.reshape(chips, cores, -1, rows.shape[-1])
    blocks = lax.all_to_all(blocks, "k", split_axis=1, concat_axis=1, tiled=True)
    blocks = lax.all_to_all(blocks, "z", split_axis=0, concat_axis=0, tiled=True)
    return blocks.reshape(rows.shape)


def around(value, steps):
    count = lax.axis_size("q")
    return lax.ppermute(value, "q", [(source, (source + steps) % count) for source in range(count)])


def silu_slope(values):
    logistic = jax.nn.sigmoid(values)
    return logistic * (1.0 + values * (1.0 - logistic))


def contract_last(first_operand, second_operand):
    return lax.dot_general(
        first_operand, second_operand, (((1,), (1,)), ((), ())), preferred_element_type=jnp.float32
    )


def local(
    route_ids,
    route_probs,
    moe_grad,
    saved_gate,
    saved_up,
    w_up,
    w_down,
    conv_grad,
    conv_pre,
    conv_kernel,
    w_key,
):
    ctx_count = lax.axis_size(CTX)
    groups = lax.axis_size("g")
    split = lax.axis_size("q")
    my_group = lax.axis_index("g")
    my_quarter = lax.axis_index("q")
    tok_rows, top_count = route_ids.shape
    features = moe_grad.shape[1]
    capacity = saved_gate.shape[2]
    slot_count = ctx_count * capacity
    expert_count = ctx_count * groups
    tap_count = conv_kernel.shape[0]
    grad_pre = conv_grad.astype(jnp.float32) * silu_slope(conv_pre.astype(jnp.float32))
    following = passed_along(grad_pre[: tap_count - 1], CTX, -1)
    extended = jnp.concatenate([grad_pre, following], 0)
    key_sum = conv_kernel[0][None, :] * extended[0:tok_rows]
    for offset in range(1, tap_count):
        key_sum = key_sum + conv_kernel[offset][None, :] * extended[offset : offset + tok_rows]
    key_grad = key_sum.astype(jnp.bfloat16)
    flat_ids = route_ids.reshape(-1)
    expert_hot = (flat_ids[:, None] == jnp.arange(expert_count, dtype=jnp.int32)[None, :]).astype(
        jnp.int32
    )
    earlier = jnp.cumsum(expert_hot, 0) - expert_hot
    arrival = jnp.sum(earlier * expert_hot, 1)
    expert_group = flat_ids % groups
    slot_index = flat_ids // groups * capacity + arrival
    own_slot = jnp.where(expert_group == my_group, slot_index, -1).reshape(tok_rows, top_count)
    own_hit = own_slot[:, :, None] == jnp.arange(slot_count, dtype=jnp.int32)[None, None, :]
    placement = jnp.sum(own_hit.astype(jnp.float32), 1).astype(jnp.bfloat16)
    slot_probs = jnp.sum(jnp.where(own_hit, route_probs[:, :, None], 0.0), (0, 1))
    chunk = features // split
    grad_chunk = lax.dynamic_slice_in_dim(moe_grad, my_quarter * chunk, chunk, axis=1)
    picked = lax.dot_general(
        placement, grad_chunk, (((0,), (0,)), ((), ())), preferred_element_type=jnp.float32
    )
    scaled_rows = (slot_probs[:, None] * picked).astype(jnp.bfloat16)
    key_grad, scaled_rows = lax.optimization_barrier((key_grad, scaled_rows))
    key_all = lax.all_gather(key_grad, "q", axis=1, tiled=True)
    key_all = lax.all_gather(key_all, "g", axis=1, tiled=True)
    hidden = w_down.shape[1]
    block = features // (groups * split)
    down_own = w_down[0].reshape(hidden, split, chunk)
    up_own = w_up[0].reshape(groups, split, block, hidden)

    def down_slice(index):
        return lax.dynamic_index_in_dim(down_own, index, 1, keepdims=False)

    def up_slice(index):
        return lax.dynamic_index_in_dim(up_own, index, 1, keepdims=False).reshape(chunk, hidden)

    down_got = [down_slice(my_quarter)]
    up_got = [up_slice(my_quarter)]
    for shift in range(1, split):
        down_got.append(around(down_slice((my_quarter + shift) % split), shift))
        up_got.append(around(up_slice((my_quarter + shift) % split), shift))
    by_block = (my_quarter - jnp.arange(split)) % split
    down_got = jnp.take(jnp.stack(down_got), by_block, axis=0)
    up_got = jnp.take(jnp.stack(up_got), by_block, axis=0)
    got_rows = across_ctx(scaled_rows)
    key_all, down_got, up_got, got_rows = lax.optimization_barrier(
        (key_all, down_got, up_got, got_rows)
    )
    key_input = contract_last(key_all, w_key)
    gate_pre = saved_gate.reshape(slot_count, -1).astype(jnp.float32)
    up_output = saved_up.reshape(slot_count, -1).astype(jnp.float32)
    hidden_parts = jnp.einsum(
        "sf,qhf->qsh", got_rows, down_got, preferred_element_type=jnp.float32
    ).astype(jnp.bfloat16)
    hidden_parts = lax.all_to_all(hidden_parts, "q", 0, 0, tiled=True)
    hidden_grad = jnp.sum(hidden_parts.astype(jnp.float32), 0)
    gate_grad = (hidden_grad * up_output * silu_slope(gate_pre)).astype(jnp.bfloat16)
    up_grad = (hidden_grad * jax.nn.silu(gate_pre)).astype(jnp.bfloat16)
    up_all = jnp.broadcast_to(up_grad[None], (split, *up_grad.shape))
    up_all = lax.all_to_all(up_all, "q", 0, 0, tiled=True)
    summed_rows = jnp.einsum(
        "qsh,qfh->sf", up_all, up_got, preferred_element_type=jnp.float32
    ).astype(jnp.bfloat16)
    came_back = across_ctx(summed_rows)
    token_rows = jnp.dot(placement, came_back, preferred_element_type=jnp.float32)
    token_rows = lax.all_to_all(token_rows.reshape(tok_rows, groups, -1), "g", 1, 1, tiled=True)
    moe_share = jnp.sum(token_rows, 1)
    input_grad = moe_share + key_input
    return (input_grad, gate_grad.reshape(saved_gate.shape))


def solution(mesh):
    ctx_count, exp_count = mesh.devices.shape
    split_mesh = Mesh(
        mesh.devices.reshape(ctx_count // CORES, CORES, exp_count // SPLIT, SPLIT),
        (*CTX, "g", "q"),
    )
    exp = ("g", "q")
    return jax.shard_map(
        local,
        mesh=split_mesh,
        in_specs=(
            P(CTX, None),
            P(CTX, None),
            P(CTX, None),
            P((*CTX, *exp), None, None, None),
            P((*CTX, *exp), None, None, None),
            P((*CTX, *exp), None, None),
            P((*CTX, *exp), None, None),
            P(CTX, exp),
            P(CTX, exp),
            P(None, exp),
            P(exp, None),
        ),
        out_specs=(P(CTX, exp), P((*CTX, *exp), None, None, None)),
        check_vma=False,
    )
```

```python
import jax
import jax.numpy as jnp
from jax import lax
from jax.sharding import Mesh
from jax.sharding import PartitionSpec as P

SPLIT = 4
CORES = 2
CTX = ("z", "k")


def passed_along(value, axis, steps):
    count = lax.axis_size(axis)
    leading, last = (max(0, -steps), min(count, count - steps))
    return lax.ppermute(value, axis, [(source, source + steps) for source in range(leading, last)])


def across_ctx(rows):
    chips, cores = lax.axis_size("z"), lax.axis_size("k")
    blocks = rows.reshape(chips, cores, -1, rows.shape[-1])
    blocks = lax.all_to_all(blocks, "k", split_axis=1, concat_axis=1, tiled=True)
    blocks = lax.all_to_all(blocks, "z", split_axis=0, concat_axis=0, tiled=True)
    return blocks.reshape(rows.shape)


def around(value, steps):
    count = lax.axis_size("q")
    return lax.ppermute(value, "q", [(source, (source + steps) % count) for source in range(count)])


def silu_slope(values):
    logistic = jax.nn.sigmoid(values)
    return logistic * (1.0 + values * (1.0 - logistic))


def contract_last(first_operand, second_operand):
    return lax.dot_general(
        first_operand, second_operand, (((1,), (1,)), ((), ())), preferred_element_type=jnp.float32
    )


def local(
    route_ids,
    route_probs,
    moe_grad,
    saved_gate,
    saved_up,
    w_up,
    w_down,
    conv_grad,
    conv_pre,
    conv_kernel,
    w_key,
):
    ctx_count = lax.axis_size(CTX)
    groups = lax.axis_size("g")
    split = lax.axis_size("q")
    my_group = lax.axis_index("g")
    my_quarter = lax.axis_index("q")
    tok_rows, top_count = route_ids.shape
    features = moe_grad.shape[1]
    capacity = saved_gate.shape[2]
    slot_count = ctx_count * capacity
    expert_count = ctx_count * groups
    tap_count = conv_kernel.shape[0]
    grad_pre = conv_grad.astype(jnp.float32) * silu_slope(conv_pre.astype(jnp.float32))
    following = passed_along(grad_pre[: tap_count - 1], CTX, -1)
    extended = jnp.concatenate([grad_pre, following], 0)
    key_sum = conv_kernel[0][None, :] * extended[0:tok_rows]
    for offset in range(1, tap_count):
        key_sum = key_sum + conv_kernel[offset][None, :] * extended[offset : offset + tok_rows]
    key_grad = key_sum.astype(jnp.bfloat16)
    flat_ids = route_ids.reshape(-1)
    expert_hot = (flat_ids[:, None] == jnp.arange(expert_count, dtype=jnp.int32)[None, :]).astype(
        jnp.int32
    )
    earlier = jnp.cumsum(expert_hot, 0) - expert_hot
    arrival = jnp.sum(earlier * expert_hot, 1)
    expert_group = flat_ids % groups
    slot_index = flat_ids // groups * capacity + arrival
    own_slot = jnp.where(expert_group == my_group, slot_index, -1).reshape(tok_rows, top_count)
    own_hit = own_slot[:, :, None] == jnp.arange(slot_count, dtype=jnp.int32)[None, None, :]
    placement = jnp.sum(own_hit.astype(jnp.float32), 1).astype(jnp.bfloat16)
    slot_probs = jnp.sum(jnp.where(own_hit, route_probs[:, :, None], 0.0), (0, 1))
    chunk = features // split
    grad_chunk = lax.dynamic_slice_in_dim(moe_grad, my_quarter * chunk, chunk, axis=1)
    picked = lax.dot_general(
        placement, grad_chunk, (((0,), (0,)), ((), ())), preferred_element_type=jnp.float32
    )
    scaled_rows = (slot_probs[:, None] * picked).astype(jnp.bfloat16)
    hidden = w_down.shape[1]
    block = features // (groups * split)
    down_own = w_down[0].reshape(hidden, split, chunk)
    up_own = w_up[0].reshape(groups, split, block, hidden)

    def down_slice(index):
        return lax.dynamic_index_in_dim(down_own, index, 1, keepdims=False)

    def up_slice(index):
        return lax.dynamic_index_in_dim(up_own, index, 1, keepdims=False).reshape(chunk, hidden)

    down_got = [down_slice(my_quarter)]
    up_got = [up_slice(my_quarter)]
    for shift in range(1, split):
        down_got.append(around(down_slice((my_quarter + shift) % split), shift))
        up_got.append(around(up_slice((my_quarter + shift) % split), shift))
    by_block = (my_quarter - jnp.arange(split)) % split
    down_got = jnp.take(jnp.stack(down_got), by_block, axis=0)
    up_got = jnp.take(jnp.stack(up_got), by_block, axis=0)
    got_rows = across_ctx(scaled_rows)
    down_got, up_got, got_rows = lax.optimization_barrier((down_got, up_got, got_rows))
    gate_pre = saved_gate.reshape(slot_count, -1).astype(jnp.float32)
    up_output = saved_up.reshape(slot_count, -1).astype(jnp.float32)
    hidden_parts = jnp.einsum(
        "sf,qhf->qsh", got_rows, down_got, preferred_element_type=jnp.float32
    ).astype(jnp.bfloat16)
    hidden_parts = lax.all_to_all(hidden_parts, "q", 0, 0, tiled=True)
    hidden_grad = jnp.sum(hidden_parts.astype(jnp.float32), 0)
    gate_grad = (hidden_grad * up_output * silu_slope(gate_pre)).astype(jnp.bfloat16)
    up_grad = (hidden_grad * jax.nn.silu(gate_pre)).astype(jnp.bfloat16)
    up_all = jnp.broadcast_to(up_grad[None], (split, *up_grad.shape))
    up_all = lax.all_to_all(up_all, "q", 0, 0, tiled=True)
    summed_rows = jnp.einsum(
        "qsh,qfh->sf", up_all, up_got, preferred_element_type=jnp.float32
    ).astype(jnp.bfloat16)
    key_grad, summed_rows = lax.optimization_barrier((key_grad, summed_rows))
    key_group = lax.all_gather(key_grad, "q", axis=1, tiled=True)
    key_got = [key_group]
    for shift in range(1, groups):
        key_got.append(
            lax.ppermute(key_group, "g", [(i, (i + shift) % groups) for i in range(groups)])
        )
    came_back = across_ctx(summed_rows)
    key_got, came_back = lax.optimization_barrier((key_got, came_back))
    key_got = jnp.take(jnp.stack(key_got), (my_group - jnp.arange(groups)) % groups, axis=0)
    key_input = jnp.einsum(
        "gtc,fgc->tf",
        key_got,
        w_key.reshape(w_key.shape[0], groups, -1),
        preferred_element_type=jnp.float32,
    )
    token_rows = jnp.dot(placement, came_back, preferred_element_type=jnp.float32)
    token_rows = lax.all_to_all(token_rows.reshape(tok_rows, groups, -1), "g", 1, 1, tiled=True)
    moe_share = jnp.sum(token_rows, 1)
    input_grad = moe_share + key_input
    return (input_grad, gate_grad.reshape(saved_gate.shape))


def solution(mesh):
    ctx_count, exp_count = mesh.devices.shape
    split_mesh = Mesh(
        mesh.devices.reshape(ctx_count // CORES, CORES, exp_count // SPLIT, SPLIT),
        (*CTX, "g", "q"),
    )
    exp = ("g", "q")
    return jax.shard_map(
        local,
        mesh=split_mesh,
        in_specs=(
            P(CTX, None),
            P(CTX, None),
            P(CTX, None),
            P((*CTX, *exp), None, None, None),
            P((*CTX, *exp), None, None, None),
            P((*CTX, *exp), None, None),
            P((*CTX, *exp), None, None),
            P(CTX, exp),
            P(CTX, exp),
            P(None, exp),
            P(exp, None),
        ),
        out_specs=(P(CTX, exp), P((*CTX, *exp), None, None, None)),
        check_vma=False,
    )
```

```python
import jax
import jax.numpy as jnp
from jax import lax
from jax.sharding import Mesh
from jax.sharding import PartitionSpec as P

SPLIT = 4
CORES = 2
CTX = ("z", "k")


def passed_along(value, axis, steps):
    count = lax.axis_size(axis)
    leading, last = (max(0, -steps), min(count, count - steps))
    return lax.ppermute(value, axis, [(source, source + steps) for source in range(leading, last)])


def across_ctx(rows):
    chips, cores = lax.axis_size("z"), lax.axis_size("k")
    blocks = rows.reshape(chips, cores, -1, rows.shape[-1])
    blocks = lax.all_to_all(blocks, "k", split_axis=1, concat_axis=1, tiled=True)
    blocks = lax.all_to_all(blocks, "z", split_axis=0, concat_axis=0, tiled=True)
    return blocks.reshape(rows.shape)


def around(value, steps):
    count = lax.axis_size("q")
    return lax.ppermute(value, "q", [(source, (source + steps) % count) for source in range(count)])


def silu_slope(values):
    logistic = jax.nn.sigmoid(values)
    return logistic * (1.0 + values * (1.0 - logistic))


def contract_last(first_operand, second_operand):
    return lax.dot_general(
        first_operand, second_operand, (((1,), (1,)), ((), ())), preferred_element_type=jnp.float32
    )


def local(
    route_ids,
    route_probs,
    moe_grad,
    saved_gate,
    saved_up,
    w_up,
    w_down,
    conv_grad,
    conv_pre,
    conv_kernel,
    w_key,
):
    ctx_count = lax.axis_size(CTX)
    groups = lax.axis_size("g")
    split = lax.axis_size("q")
    my_group = lax.axis_index("g")
    my_quarter = lax.axis_index("q")
    tok_rows, top_count = route_ids.shape
    features = moe_grad.shape[1]
    capacity = saved_gate.shape[2]
    slot_count = ctx_count * capacity
    expert_count = ctx_count * groups
    tap_count = conv_kernel.shape[0]
    grad_pre = conv_grad.astype(jnp.float32) * silu_slope(conv_pre.astype(jnp.float32))
    following = passed_along(grad_pre[: tap_count - 1], CTX, -1)
    extended = jnp.concatenate([grad_pre, following], 0)
    key_sum = conv_kernel[0][None, :] * extended[0:tok_rows]
    for offset in range(1, tap_count):
        key_sum = key_sum + conv_kernel[offset][None, :] * extended[offset : offset + tok_rows]
    key_grad = key_sum.astype(jnp.bfloat16)
    flat_ids = route_ids.reshape(-1)
    expert_hot = (flat_ids[:, None] == jnp.arange(expert_count, dtype=jnp.int32)[None, :]).astype(
        jnp.int32
    )
    earlier = jnp.cumsum(expert_hot, 0) - expert_hot
    arrival = jnp.sum(earlier * expert_hot, 1)
    expert_group = flat_ids % groups
    slot_index = flat_ids // groups * capacity + arrival
    own_slot = jnp.where(expert_group == my_group, slot_index, -1).reshape(tok_rows, top_count)
    own_hit = own_slot[:, :, None] == jnp.arange(slot_count, dtype=jnp.int32)[None, None, :]
    placement = jnp.sum(own_hit.astype(jnp.float32), 1).astype(jnp.bfloat16)
    slot_probs = jnp.sum(jnp.where(own_hit, route_probs[:, :, None], 0.0), (0, 1))
    chunk = features // split
    grad_chunk = lax.dynamic_slice_in_dim(moe_grad, my_quarter * chunk, chunk, axis=1)
    picked = lax.dot_general(
        placement, grad_chunk, (((0,), (0,)), ((), ())), preferred_element_type=jnp.float32
    )
    scaled_rows = (slot_probs[:, None] * picked).astype(jnp.bfloat16)
    hidden = w_down.shape[1]
    block = features // (groups * split)
    down_own = w_down[0].reshape(hidden, split, chunk)
    up_own = w_up[0].reshape(groups, split, block, hidden)

    def down_slice(index):
        return lax.dynamic_index_in_dim(down_own, index, 1, keepdims=False)

    def up_slice(index):
        return lax.dynamic_index_in_dim(up_own, index, 1, keepdims=False).reshape(chunk, hidden)

    down_got = [down_slice(my_quarter)]
    up_got = [up_slice(my_quarter)]
    for shift in range(1, split):
        down_got.append(around(down_slice((my_quarter + shift) % split), shift))
        up_got.append(around(up_slice((my_quarter + shift) % split), shift))
    by_block = (my_quarter - jnp.arange(split)) % split
    down_got = jnp.take(jnp.stack(down_got), by_block, axis=0)
    up_got = jnp.take(jnp.stack(up_got), by_block, axis=0)
    got_rows = across_ctx(scaled_rows)
    key_grad, down_got, up_got, got_rows = lax.optimization_barrier(
        (key_grad, down_got, up_got, got_rows)
    )
    gate_pre = saved_gate.reshape(slot_count, -1).astype(jnp.float32)
    up_output = saved_up.reshape(slot_count, -1).astype(jnp.float32)
    hidden_parts = jnp.einsum(
        "sf,qhf->qsh", got_rows, down_got, preferred_element_type=jnp.float32
    ).astype(jnp.bfloat16)
    hidden_parts = lax.all_to_all(hidden_parts, "q", 0, 0, tiled=True)
    hidden_grad = jnp.sum(hidden_parts.astype(jnp.float32), 0)
    gate_grad = (hidden_grad * up_output * silu_slope(gate_pre)).astype(jnp.bfloat16)
    up_grad = (hidden_grad * jax.nn.silu(gate_pre)).astype(jnp.bfloat16)
    up_all = jnp.broadcast_to(up_grad[None], (split, *up_grad.shape))
    up_all = lax.all_to_all(up_all, "q", 0, 0, tiled=True)
    summed_rows = jnp.einsum(
        "qsh,qfh->sf", up_all, up_got, preferred_element_type=jnp.float32
    ).astype(jnp.bfloat16)
    key_grad, summed_rows = lax.optimization_barrier((key_grad, summed_rows))
    key_group = lax.all_gather(key_grad, "q", axis=1, tiled=True)
    key_got = [key_group]
    for shift in range(1, groups):
        key_got.append(
            lax.ppermute(key_group, "g", [(i, (i + shift) % groups) for i in range(groups)])
        )
    came_back = across_ctx(summed_rows)
    key_got, came_back = lax.optimization_barrier((key_got, came_back))
    key_got = jnp.take(jnp.stack(key_got), (my_group - jnp.arange(groups)) % groups, axis=0)
    key_input = jnp.einsum(
        "gtc,fgc->tf",
        key_got,
        w_key.reshape(w_key.shape[0], groups, -1),
        preferred_element_type=jnp.float32,
    )
    token_rows = jnp.dot(placement, came_back, preferred_element_type=jnp.float32)
    token_rows = lax.all_to_all(token_rows.reshape(tok_rows, groups, -1), "g", 1, 1, tiled=True)
    moe_share = jnp.sum(token_rows, 1)
    input_grad = moe_share + key_input
    return (input_grad, gate_grad.reshape(saved_gate.shape))


def solution(mesh):
    ctx_count, exp_count = mesh.devices.shape
    split_mesh = Mesh(
        mesh.devices.reshape(ctx_count // CORES, CORES, exp_count // SPLIT, SPLIT),
        (*CTX, "g", "q"),
    )
    exp = ("g", "q")
    return jax.shard_map(
        local,
        mesh=split_mesh,
        in_specs=(
            P(CTX, None),
            P(CTX, None),
            P(CTX, None),
            P((*CTX, *exp), None, None, None),
            P((*CTX, *exp), None, None, None),
            P((*CTX, *exp), None, None),
            P((*CTX, *exp), None, None),
            P(CTX, exp),
            P(CTX, exp),
            P(None, exp),
            P(exp, None),
        ),
        out_specs=(P(CTX, exp), P((*CTX, *exp), None, None, None)),
        check_vma=False,
    )
```

```python
import jax
import jax.numpy as jnp
from jax import lax
from jax.sharding import Mesh
from jax.sharding import PartitionSpec as P

SPLIT = 4
CORES = 2
CTX = ("z", "k")


def passed_along(value, axis, steps):
    count = lax.axis_size(axis)
    leading, last = (max(0, -steps), min(count, count - steps))
    return lax.ppermute(value, axis, [(source, source + steps) for source in range(leading, last)])


def across_ctx(rows):
    chips, cores = lax.axis_size("z"), lax.axis_size("k")
    blocks = rows.reshape(chips, cores, -1, rows.shape[-1])
    blocks = lax.all_to_all(blocks, "k", split_axis=1, concat_axis=1, tiled=True)
    blocks = lax.all_to_all(blocks, "z", split_axis=0, concat_axis=0, tiled=True)
    return blocks.reshape(rows.shape)


def around(value, steps):
    count = lax.axis_size("q")
    return lax.ppermute(value, "q", [(source, (source + steps) % count) for source in range(count)])


def silu_slope(values):
    logistic = jax.nn.sigmoid(values)
    return logistic * (1.0 + values * (1.0 - logistic))


def contract_last(first_operand, second_operand):
    return lax.dot_general(
        first_operand, second_operand, (((1,), (1,)), ((), ())), preferred_element_type=jnp.float32
    )


def local(
    route_ids,
    route_probs,
    moe_grad,
    saved_gate,
    saved_up,
    w_up,
    w_down,
    conv_grad,
    conv_pre,
    conv_kernel,
    w_key,
):
    ctx_count = lax.axis_size(CTX)
    groups = lax.axis_size("g")
    split = lax.axis_size("q")
    my_group = lax.axis_index("g")
    my_quarter = lax.axis_index("q")
    tok_rows, top_count = route_ids.shape
    features = moe_grad.shape[1]
    capacity = saved_gate.shape[2]
    slot_count = ctx_count * capacity
    expert_count = ctx_count * groups
    tap_count = conv_kernel.shape[0]
    grad_pre = conv_grad.astype(jnp.float32) * silu_slope(conv_pre.astype(jnp.float32))
    following = passed_along(grad_pre[: tap_count - 1], CTX, -1)
    extended = jnp.concatenate([grad_pre, following], 0)
    key_sum = conv_kernel[0][None, :] * extended[0:tok_rows]
    for offset in range(1, tap_count):
        key_sum = key_sum + conv_kernel[offset][None, :] * extended[offset : offset + tok_rows]
    key_grad = key_sum.astype(jnp.bfloat16)
    flat_ids = route_ids.reshape(-1)
    expert_hot = (flat_ids[:, None] == jnp.arange(expert_count, dtype=jnp.int32)[None, :]).astype(
        jnp.int32
    )
    earlier = jnp.cumsum(expert_hot, 0) - expert_hot
    arrival = jnp.sum(earlier * expert_hot, 1)
    expert_group = flat_ids % groups
    slot_index = flat_ids // groups * capacity + arrival
    own_slot = jnp.where(expert_group == my_group, slot_index, -1).reshape(tok_rows, top_count)
    own_hit = own_slot[:, :, None] == jnp.arange(slot_count, dtype=jnp.int32)[None, None, :]
    placement = jnp.sum(own_hit.astype(jnp.float32), 1).astype(jnp.bfloat16)
    slot_probs = jnp.sum(jnp.where(own_hit, route_probs[:, :, None], 0.0), (0, 1))
    chunk = features // split
    grad_chunk = lax.dynamic_slice_in_dim(moe_grad, my_quarter * chunk, chunk, axis=1)
    picked = lax.dot_general(
        placement, grad_chunk, (((0,), (0,)), ((), ())), preferred_element_type=jnp.float32
    )
    scaled_rows = (slot_probs[:, None] * picked).astype(jnp.bfloat16)
    hidden = w_down.shape[1]
    block = features // (groups * split)
    down_own = w_down[0].reshape(hidden, split, chunk)
    up_own = w_up[0].reshape(groups, split, block, hidden)

    def down_slice(index):
        return lax.dynamic_index_in_dim(down_own, index, 1, keepdims=False)

    def up_slice(index):
        return lax.dynamic_index_in_dim(up_own, index, 1, keepdims=False).reshape(chunk, hidden)

    down_got = [down_slice(my_quarter)]
    up_got = [up_slice(my_quarter)]
    for shift in range(1, split):
        down_got.append(around(down_slice((my_quarter + shift) % split), shift))
        up_got.append(around(up_slice((my_quarter + shift) % split), shift))
    by_block = (my_quarter - jnp.arange(split)) % split
    down_got = jnp.take(jnp.stack(down_got), by_block, axis=0)
    up_got = jnp.take(jnp.stack(up_got), by_block, axis=0)
    got_rows = across_ctx(scaled_rows)
    down_got, up_got, got_rows = lax.optimization_barrier((down_got, up_got, got_rows))
    gate_pre = saved_gate.reshape(slot_count, -1).astype(jnp.float32)
    up_output = saved_up.reshape(slot_count, -1).astype(jnp.float32)
    hidden_parts = jnp.einsum(
        "sf,qhf->qsh", got_rows, down_got, preferred_element_type=jnp.float32
    ).astype(jnp.bfloat16)
    hidden_parts = lax.all_to_all(hidden_parts, "q", 0, 0, tiled=True)
    hidden_grad = jnp.sum(hidden_parts.astype(jnp.float32), 0)
    gate_grad = (hidden_grad * up_output * silu_slope(gate_pre)).astype(jnp.bfloat16)
    up_grad = (hidden_grad * jax.nn.silu(gate_pre)).astype(jnp.bfloat16)
    up_all = jnp.broadcast_to(up_grad[None], (split, *up_grad.shape))
    up_all = lax.all_to_all(up_all, "q", 0, 0, tiled=True)
    summed_rows = jnp.einsum(
        "qsh,qfh->sf", up_all, up_got, preferred_element_type=jnp.float32
    ).astype(jnp.bfloat16)
    key_grad, summed_rows = lax.optimization_barrier((key_grad, summed_rows))
    key_group = lax.all_gather(key_grad, "q", axis=1, tiled=True)
    key_got = [key_group]
    for shift in range(1, groups):
        key_got.append(
            lax.ppermute(key_group, "g", [(i, (i + shift) % groups) for i in range(groups)])
        )
    came_back = across_ctx(summed_rows)
    key_got, came_back = lax.optimization_barrier((key_got, came_back))
    key_got = jnp.take(jnp.stack(key_got), (my_group - jnp.arange(groups)) % groups, axis=0)
    key_input = jnp.einsum(
        "gtc,fgc->tf",
        key_got,
        w_key.reshape(w_key.shape[0], groups, -1),
        preferred_element_type=jnp.float32,
    )
    token_rows = jnp.dot(placement, came_back, preferred_element_type=jnp.float32)
    token_rows = token_rows.astype(jnp.bfloat16).reshape(tok_rows, groups, -1)
    token_rows = lax.all_to_all(token_rows, "g", 1, 1, tiled=True)
    moe_share = jnp.sum(token_rows.astype(jnp.float32), 1)
    input_grad = moe_share + key_input
    return (input_grad, gate_grad.reshape(saved_gate.shape))


def solution(mesh):
    ctx_count, exp_count = mesh.devices.shape
    split_mesh = Mesh(
        mesh.devices.reshape(ctx_count // CORES, CORES, exp_count // SPLIT, SPLIT),
        (*CTX, "g", "q"),
    )
    exp = ("g", "q")
    return jax.shard_map(
        local,
        mesh=split_mesh,
        in_specs=(
            P(CTX, None),
            P(CTX, None),
            P(CTX, None),
            P((*CTX, *exp), None, None, None),
            P((*CTX, *exp), None, None, None),
            P((*CTX, *exp), None, None),
            P((*CTX, *exp), None, None),
            P(CTX, exp),
            P(CTX, exp),
            P(None, exp),
            P(exp, None),
        ),
        out_specs=(P(CTX, exp), P((*CTX, *exp), None, None, None)),
        check_vma=False,
    )
```

```python
import jax
import jax.numpy as jnp
from jax import lax
from jax.sharding import Mesh
from jax.sharding import PartitionSpec as P

SPLIT = 4
CORES = 2
CTX = ("z", "k")


def passed_along(value, axis, steps):
    count = lax.axis_size(axis)
    leading, last = (max(0, -steps), min(count, count - steps))
    return lax.ppermute(value, axis, [(source, source + steps) for source in range(leading, last)])


def across_ctx(rows):
    chips, cores = lax.axis_size("z"), lax.axis_size("k")
    blocks = rows.reshape(chips, cores, -1, rows.shape[-1])
    blocks = lax.all_to_all(blocks, "k", split_axis=1, concat_axis=1, tiled=True)
    blocks = lax.all_to_all(blocks, "z", split_axis=0, concat_axis=0, tiled=True)
    return blocks.reshape(rows.shape)


def around(value, steps):
    count = lax.axis_size("q")
    return lax.ppermute(value, "q", [(source, (source + steps) % count) for source in range(count)])


def silu_slope(values):
    logistic = jax.nn.sigmoid(values)
    return logistic * (1.0 + values * (1.0 - logistic))


def contract_last(first_operand, second_operand):
    return lax.dot_general(
        first_operand, second_operand, (((1,), (1,)), ((), ())), preferred_element_type=jnp.float32
    )


def local(
    route_ids,
    route_probs,
    moe_grad,
    saved_gate,
    saved_up,
    w_up,
    w_down,
    conv_grad,
    conv_pre,
    conv_kernel,
    w_key,
):
    ctx_count = lax.axis_size(CTX)
    groups = lax.axis_size("g")
    split = lax.axis_size("q")
    my_group = lax.axis_index("g")
    my_quarter = lax.axis_index("q")
    tok_rows, top_count = route_ids.shape
    features = moe_grad.shape[1]
    capacity = saved_gate.shape[2]
    slot_count = ctx_count * capacity
    expert_count = ctx_count * groups
    tap_count = conv_kernel.shape[0]
    grad_pre = conv_grad.astype(jnp.float32) * silu_slope(conv_pre.astype(jnp.float32))
    following = passed_along(grad_pre[: tap_count - 1], CTX, -1)
    extended = jnp.concatenate([grad_pre, following], 0)
    key_sum = conv_kernel[0][None, :] * extended[0:tok_rows]
    for offset in range(1, tap_count):
        key_sum = key_sum + conv_kernel[offset][None, :] * extended[offset : offset + tok_rows]
    key_grad = key_sum.astype(jnp.bfloat16)
    flat_ids = route_ids.reshape(-1)
    expert_hot = (flat_ids[:, None] == jnp.arange(expert_count, dtype=jnp.int32)[None, :]).astype(
        jnp.int32
    )
    earlier = jnp.cumsum(expert_hot, 0) - expert_hot
    arrival = jnp.sum(earlier * expert_hot, 1)
    expert_group = flat_ids % groups
    slot_index = flat_ids // groups * capacity + arrival
    own_slot = jnp.where(expert_group == my_group, slot_index, -1).reshape(tok_rows, top_count)
    own_hit = own_slot[:, :, None] == jnp.arange(slot_count, dtype=jnp.int32)[None, None, :]
    placement = jnp.sum(own_hit.astype(jnp.float32), 1).astype(jnp.bfloat16)
    slot_probs = jnp.sum(jnp.where(own_hit, route_probs[:, :, None], 0.0), (0, 1))
    chunk = features // split
    grad_chunk = lax.dynamic_slice_in_dim(moe_grad, my_quarter * chunk, chunk, axis=1)
    picked = lax.dot_general(
        placement, grad_chunk, (((0,), (0,)), ((), ())), preferred_element_type=jnp.float32
    )
    scaled_rows = (slot_probs[:, None] * picked).astype(jnp.bfloat16)
    hidden = w_down.shape[1]
    block = features // (groups * split)
    down_own = w_down[0].reshape(hidden, split, chunk)
    up_own = w_up[0].reshape(groups, split, block, hidden)

    def down_slice(index):
        return lax.dynamic_index_in_dim(down_own, index, 1, keepdims=False)

    def up_slice(index):
        return lax.dynamic_index_in_dim(up_own, index, 1, keepdims=False).reshape(chunk, hidden)

    down_got = [down_slice(my_quarter)]
    up_got = [up_slice(my_quarter)]
    for shift in range(1, split):
        down_got.append(around(down_slice((my_quarter + shift) % split), shift))
        up_got.append(around(up_slice((my_quarter + shift) % split), shift))
    by_block = (my_quarter - jnp.arange(split)) % split
    down_got = jnp.take(jnp.stack(down_got), by_block, axis=0)
    up_got = jnp.take(jnp.stack(up_got), by_block, axis=0)
    got_rows = across_ctx(scaled_rows)
    down_got, up_got, got_rows = lax.optimization_barrier((down_got, up_got, got_rows))
    gate_pre = saved_gate.reshape(slot_count, -1).astype(jnp.float32)
    up_output = saved_up.reshape(slot_count, -1).astype(jnp.float32)
    hidden_parts = jnp.einsum(
        "sf,qhf->qsh", got_rows, down_got, preferred_element_type=jnp.float32
    ).astype(jnp.bfloat16)
    hidden_parts = lax.all_to_all(hidden_parts, "q", 0, 0, tiled=True)
    hidden_grad = jnp.sum(hidden_parts.astype(jnp.float32), 0)
    gate_grad = (hidden_grad * up_output * silu_slope(gate_pre)).astype(jnp.bfloat16)
    up_grad = (hidden_grad * jax.nn.silu(gate_pre)).astype(jnp.bfloat16)
    up_all = jnp.broadcast_to(up_grad[None], (split, *up_grad.shape))
    up_all = lax.all_to_all(up_all, "q", 0, 0, tiled=True)
    summed_rows = jnp.einsum(
        "qsh,qfh->sf", up_all, up_got, preferred_element_type=jnp.float32
    ).astype(jnp.bfloat16)
    key_weights = jnp.take(
        w_key.reshape(w_key.shape[0], groups, -1), (my_group - jnp.arange(groups)) % groups, axis=1
    )
    key_grad, key_weights, summed_rows = lax.optimization_barrier(
        (key_grad, key_weights, summed_rows)
    )
    key_group = lax.all_gather(key_grad, "q", axis=1, tiled=True)
    key_got = [key_group]
    for shift in range(1, groups):
        key_got.append(
            lax.ppermute(key_group, "g", [(i, (i + shift) % groups) for i in range(groups)])
        )
    came_back = across_ctx(summed_rows)
    key_got, came_back = lax.optimization_barrier((key_got, came_back))
    key_input = jnp.einsum(
        "gtc,fgc->tf",
        jnp.stack(key_got),
        key_weights,
        preferred_element_type=jnp.float32,
    )
    token_rows = jnp.dot(placement, came_back, preferred_element_type=jnp.float32)
    token_rows = token_rows.astype(jnp.bfloat16).reshape(tok_rows, groups, -1)
    token_rows = lax.all_to_all(token_rows, "g", 1, 1, tiled=True)
    moe_share = jnp.sum(token_rows.astype(jnp.float32), 1)
    input_grad = moe_share + key_input
    return (input_grad, gate_grad.reshape(saved_gate.shape))


def solution(mesh):
    ctx_count, exp_count = mesh.devices.shape
    split_mesh = Mesh(
        mesh.devices.reshape(ctx_count // CORES, CORES, exp_count // SPLIT, SPLIT),
        (*CTX, "g", "q"),
    )
    exp = ("g", "q")
    return jax.shard_map(
        local,
        mesh=split_mesh,
        in_specs=(
            P(CTX, None),
            P(CTX, None),
            P(CTX, None),
            P((*CTX, *exp), None, None, None),
            P((*CTX, *exp), None, None, None),
            P((*CTX, *exp), None, None),
            P((*CTX, *exp), None, None),
            P(CTX, exp),
            P(CTX, exp),
            P(None, exp),
            P(exp, None),
        ),
        out_specs=(P(CTX, exp), P((*CTX, *exp), None, None, None)),
        check_vma=False,
    )
```
